256 devices in a mesh: shard: 64 (over x, z_hi, y), rep: 4 (over z_lo, core).
Axes of the slice: x: 4, y: 4, z: 8 (z_hi: 4, z_lo: 2; z = z_hi * 2 + z_lo), core: 2. Of those that a mesh axis runs over, the one named last changes fastest.
Arguments:
- docs: bfloat16 [32768, 16384], P('shard', 'rep')
- pattern: int32 [256, 128], P('shard', 'rep'), may hold values 0 or 1
- owners: int32 [4], replicated, may hold values from 0 to 63
Outputs:
- scores: bfloat16 [4, 256, 32768], P(None, ('shard', 'rep'))
The draws below stay inside these ranges and needn't reach their ends.
All inputs are finite; a program needn't handle non-finite values. No bound on the sum of `pattern` on one device may be relied on, other than what follows from the above.
Results may differ from the reference program's by a relative error of at most 0.001.
Values may be sent and summed in bfloat16 or wider, within the bound.
No kernel may reach another device: no remote copies, remote signals or barrier semaphores. Data moves between devices by JAX's collectives and lax.ppermute only.
A program may use at most 128 MiB of HBM per device.

```python
import math
import jax
import jax.numpy as jnp
from jax import lax

TILE = 128
TERMS = 16384
DOC_DEV = 512
QUERY = 256
STEPS = 4
TILES = 128
DOCS = 32768
N_SHARD = 64


def draw_docs(key, part):
    first_key, second_key, third_key = jax.random.split(jax.random.fold_in(key, 17), 3)
    base = jnp.clip(jax.random.normal(first_key, (DOCS, TERMS), jnp.float32), -6.0, 6.0)
    row_scale = jnp.exp(jax.random.uniform(second_key, (DOCS, 1), jnp.float32) * math.log(10.0))
    column_scale = jnp.exp(jax.random.uniform(third_key, (1, TERMS), jnp.float32) * math.log(10.0))
    return (base * row_scale * column_scale).astype(jnp.bfloat16)


def plant(array, own_key, least, high):
    longest = array.shape.index(max(array.shape))
    spots = []
    for shift in (0, 1):
        where = [jax.random.randint(jax.random.fold_in(own_key, axis), (), 0, length) for axis, length in enumerate(array.shape)]
        where[longest] = (where[longest] + shift) % array.shape[longest]
        spots.append(tuple(where))
    return array.at[spots[0]].set(least).at[spots[1]].set(high)


def setup_inputs(seed: int = 0) -> dict:
    key_list = jax.random.split(jax.random.key(seed), 4)
    docs = draw_docs(jax.random.fold_in(key_list[3], 71), 0)
    pattern = plant((jax.random.randint(key_list[1], (DOCS // TILE, TILES), 0, 2) < 1).astype(jnp.int32), jax.random.fold_in(key_list[1], 1), 0, 1)
    owners = plant(jax.random.randint(key_list[2], (STEPS,), 0, N_SHARD), jax.random.fold_in(key_list[2], 1), 0, N_SHARD - 1).astype(jnp.int32)
    return {"docs": docs, "pattern": pattern, "owners": owners}


EPSILON = 1e-06
CLIP_LEVEL = 1.5

def reference(docs, pattern, owners):
    weights = pattern.astype(jnp.bfloat16)
    masked = (docs.reshape(DOCS // TILE, TILE, TILES, TILE) * weights[:, None, :, None]).reshape(DOCS, TERMS)
    by_shard = masked.reshape(N_SHARD, DOC_DEV, TERMS)

    def square_sums(block_rows):
        values = block_rows.astype(jnp.float32)
        return lax.optimization_barrier(jnp.sum(values * values, axis=1))
    doc_sq = lax.map(square_sums, by_shard).reshape(DOCS)
    inverse = lax.rsqrt(doc_sq + EPSILON)
    sharpen = math.sqrt(TERMS) * 0.5
    results = []
    for step_index in range(STEPS):
        offset = step_index % (DOC_DEV // QUERY) * QUERY
        first_row = (owners[step_index] * DOC_DEV + offset).astype(jnp.int32)
        queries = lax.dynamic_slice_in_dim(masked, first_row, QUERY, 0)
        query_inv = lax.dynamic_slice_in_dim(inverse, first_row, QUERY, 0)

        def products(block_rows):
            return lax.dot_general(queries, block_rows, (((1,), (1,)), ((), ())), preferred_element_type=jnp.float32)
        similar = lax.map(products, by_shard).transpose(1, 0, 2).reshape(QUERY, DOCS)
        scaled = similar * query_inv[:, None] * inverse[None, :] * sharpen
        results.append(jnp.clip(scaled, -CLIP_LEVEL, CLIP_LEVEL).astype(jnp.bfloat16))
    return jnp.stack(results)
```

```python
import math

import jax
import jax.numpy as jnp
from jax import lax
from jax.sharding import Mesh
from jax.sharding import PartitionSpec as P

TERMS = 16384
QUERY = 256
STEPS = 4


EPSILON = 1e-06
CLIP_LEVEL = 1.5

AX = ("x", "zh", "y")
RP = ("zl", "c")


def scatter_from_owner(cand, owners, sizes):
    steps, rows, terms = cand.shape
    nx, nz, ny = sizes
    coord = {"x": owners // (nz * ny), "zh": (owners // ny) % nz, "y": owners % ny}
    buf = cand.reshape(steps, nx, nz, ny, rows // (nx * nz * ny), terms)
    for name in ("y", "x", "zh"):
        dim = 1 + AX.index(name)
        got = lax.all_to_all(buf, name, split_axis=dim, concat_axis=dim, tiled=True)
        buf = jnp.stack(
            [lax.dynamic_slice_in_dim(got[s], coord[name][s], 1, axis=dim - 1) for s in range(steps)]
        )
    return buf.reshape(steps, rows // (nx * nz * ny), terms)


def on_device(docs, pattern, owners, sizes):
    nx, nz, ny = sizes
    n_shard = nx * nz * ny
    n_rep = lax.axis_size(RP)
    rep_index = lax.axis_index(RP)
    doc_rows, term_cols = docs.shape
    tile_edge = 128
    weights = pattern.astype(jnp.bfloat16)
    masked = (
        docs.reshape(doc_rows // tile_edge, tile_edge, term_cols // tile_edge, tile_edge)
        * weights[:, None, :, None]
    ).reshape(doc_rows, term_cols)
    partial_sq = jnp.einsum("dt,dt->d", masked, masked, preferred_element_type=jnp.float32)
    doc_sq = lax.psum(partial_sq, RP)
    inverse = lax.rsqrt(doc_sq + EPSILON)
    sharpen = math.sqrt(TERMS) * 0.5
    cands = jnp.stack(
        [masked[(s % (doc_rows // QUERY)) * QUERY :][:QUERY] for s in range(STEPS)]
    )
    pieces = scatter_from_owner(cands, owners, sizes)
    queries = lax.all_gather(pieces, AX, axis=1, tiled=True)
    q_sq = jnp.einsum("sqt,sqt->sq", queries, queries, preferred_element_type=jnp.float32)
    q_inv = lax.rsqrt(lax.psum(q_sq, RP) + EPSILON)
    similar = jnp.einsum("sqt,dt->sqd", queries, masked, preferred_element_type=jnp.float32)
    row_share = QUERY // (n_shard * n_rep)
    similar = similar.reshape(STEPS, n_shard, n_rep, row_share, doc_rows).transpose(0, 2, 1, 3, 4)
    mine = lax.psum_scatter(similar, RP, scatter_dimension=1, tiled=True)[:, 0]
    my_inv = lax.dynamic_index_in_dim(
        q_inv.reshape(STEPS, n_shard, n_rep, row_share), rep_index, 2, keepdims=False
    )
    scaled = mine * my_inv[..., None] * inverse[None, None, None, :] * sharpen
    scores = jnp.clip(scaled, -CLIP_LEVEL, CLIP_LEVEL).astype(jnp.bfloat16)
    got = lax.all_to_all(scores, AX, split_axis=1, concat_axis=1, tiled=True)
    return got.transpose(0, 2, 1, 3).reshape(STEPS, row_share, n_shard * doc_rows)


def solution(mesh):
    names = dict(zip(("x", "z_hi", "y"), (4, 4, 4)))
    n_shard, n_rep = mesh.devices.shape
    sizes = (names["x"], names["z_hi"], names["y"])
    assert sizes[0] * sizes[1] * sizes[2] == n_shard and n_rep == 4
    mesh5 = Mesh(mesh.devices.reshape(*sizes, 2, 2), AX + RP)
    return jax.shard_map(
        lambda d, p, o: on_device(d, p, o, sizes),
        mesh=mesh5,
        in_specs=(P(AX, RP), P(AX, RP), P()),
        out_specs=P(None, AX + RP, None),
        check_vma=False,
    )
```

```python
import math

import jax
import jax.numpy as jnp
from jax import lax
from jax.sharding import Mesh
from jax.sharding import PartitionSpec as P

TERMS = 16384
QUERY = 256
STEPS = 4


EPSILON = 1e-06
CLIP_LEVEL = 1.5

AX = ("x", "zh", "y")
RP = ("zl", "c")
ORDERS = (("y", "x", "zh"), ("x", "y", "zh"))


def exchange(buf, name, dim):
    return lax.all_to_all(buf, name, split_axis=dim, concat_axis=dim, tiled=True)


def broadcast_from_owner(cand, owners, sizes, order):
    steps = cand.shape[0]
    nx, nz, ny = sizes
    coord = {"x": owners // (nz * ny), "zh": (owners // ny) % nz, "y": owners % ny}
    buf = cand
    for name in order:
        dim = 1 + AX.index(name)
        got = exchange(buf, name, dim)
        buf = jnp.stack(
            [lax.dynamic_slice_in_dim(got[s], coord[name][s], 1, axis=dim - 1) for s in range(steps)]
        )
    for name in reversed(order):
        dim = 1 + AX.index(name)
        shape = list(buf.shape)
        shape[dim] = sizes[AX.index(name)]
        buf = exchange(jnp.broadcast_to(buf, shape), name, dim)
    return buf


def on_device(docs, pattern, owners, sizes):
    nx, nz, ny = sizes
    n_shard = nx * nz * ny
    n_rep = lax.axis_size(RP)
    doc_rows, term_cols = docs.shape
    tile_edge = 128
    weights = pattern.astype(jnp.bfloat16)
    masked = (
        docs.reshape(doc_rows // tile_edge, tile_edge, term_cols // tile_edge, tile_edge)
        * weights[:, None, :, None]
    ).reshape(doc_rows, term_cols)
    partial_sq = jnp.einsum("dt,dt->d", masked, masked, preferred_element_type=jnp.float32)
    doc_sq = lax.psum(partial_sq, RP)
    inverse = lax.rsqrt(doc_sq + EPSILON)
    sharpen = math.sqrt(TERMS) * 0.5
    row_piece = QUERY // n_shard
    cands = jnp.stack(
        [masked[(s % (doc_rows // QUERY)) * QUERY :][:QUERY] for s in range(STEPS)]
    ).reshape(STEPS, nx, nz, ny, row_piece, term_cols)
    share = term_cols // len(ORDERS)
    parts = [
        broadcast_from_owner(cands[..., k * share : (k + 1) * share], owners, sizes, order)
        for k, order in enumerate(ORDERS)
    ]
    queries = jnp.concatenate(parts, axis=-1).reshape(STEPS, QUERY, term_cols)
    q_sq = jnp.einsum("sqt,sqt->sq", queries, queries, preferred_element_type=jnp.float32)
    q_inv = lax.rsqrt(lax.psum(q_sq, RP) + EPSILON)
    similar = jnp.einsum("sqt,dt->sqd", queries, masked, preferred_element_type=jnp.float32)
    row_share = QUERY // (n_shard * n_rep)
    similar = similar.reshape(STEPS, n_shard, 2, 2, row_share, doc_rows).transpose(0, 2, 3, 1, 4, 5)
    similar = jnp.sum(exchange(similar, "c", 2), axis=2)
    mine = jnp.sum(exchange(similar, "zl", 1), axis=1)
    rep_index = lax.axis_index(RP)
    my_inv = lax.dynamic_index_in_dim(
        q_inv.reshape(STEPS, n_shard, n_rep, row_share), rep_index, 2, keepdims=False
    )
    scaled = mine * my_inv[..., None] * inverse[None, None, None, :] * sharpen
    scores = jnp.clip(scaled, -CLIP_LEVEL, CLIP_LEVEL).astype(jnp.bfloat16)
    scores = scores.reshape(STEPS, nx, nz, ny, row_share, doc_rows)
    for name in ("y", "x", "zh"):
        scores = exchange(scores, name, 1 + AX.index(name))
    return scores.transpose(0, 4, 1, 2, 3, 5).reshape(STEPS, row_share, n_shard * doc_rows)


def solution(mesh):
    names = dict(zip(("x", "z_hi", "y"), (4, 4, 4)))
    n_shard, n_rep = mesh.devices.shape
    sizes = (names["x"], names["z_hi"], names["y"])
    assert sizes[0] * sizes[1] * sizes[2] == n_shard and n_rep == 4
    mesh5 = Mesh(mesh.devices.reshape(*sizes, 2, 2), AX + RP)
    return jax.shard_map(
        lambda d, p, o: on_device(d, p, o, sizes),
        mesh=mesh5,
        in_specs=(P(AX, RP), P(AX, RP), P()),
        out_specs=P(None, AX + RP, None),
        check_vma=False,
    )
```

```python
import math

import jax
import jax.numpy as jnp
from jax import lax
from jax.sharding import Mesh
from jax.sharding import PartitionSpec as P

TERMS = 16384
QUERY = 256
STEPS = 4


EPSILON = 1e-06
CLIP_LEVEL = 1.5

AX = ("x", "zh", "y")
RP = ("zl", "c")
GROUPS = ((0, 1), (2, 3))


def exchange(buf, name, dim):
    return lax.all_to_all(buf, name, split_axis=dim, concat_axis=dim, tiled=True)


def scatter_from_owner(cand, owners, sizes):
    steps, rows, terms = cand.shape
    nx, nz, ny = sizes
    coord = {"x": owners // (nz * ny), "zh": (owners // ny) % nz, "y": owners % ny}
    buf = cand.reshape(steps, nx, nz, ny, rows // (nx * nz * ny), terms)
    for name in ("y", "x", "zh"):
        dim = 1 + AX.index(name)
        got = lax.all_to_all(buf, name, split_axis=dim, concat_axis=dim, tiled=True)
        buf = jnp.stack(
            [lax.dynamic_slice_in_dim(got[s], coord[name][s], 1, axis=dim - 1) for s in range(steps)]
        )
    return buf.reshape(steps, rows // (nx * nz * ny), terms)


def on_device(docs, pattern, owners, sizes):
    nx, nz, ny = sizes
    n_shard = nx * nz * ny
    n_rep = lax.axis_size(RP)
    rep_index = lax.axis_index(RP)
    doc_rows, term_cols = docs.shape
    tile_edge = 128
    weights = pattern.astype(jnp.bfloat16)
    masked = (
        docs.reshape(doc_rows // tile_edge, tile_edge, term_cols // tile_edge, tile_edge)
        * weights[:, None, :, None]
    ).reshape(doc_rows, term_cols)
    partial_sq = jnp.einsum("dt,dt->d", masked, masked, preferred_element_type=jnp.float32)
    doc_sq = lax.psum(partial_sq, RP)
    inverse = lax.rsqrt(doc_sq + EPSILON)
    sharpen = math.sqrt(TERMS) * 0.5
    row_share = QUERY // (n_shard * n_rep)
    outs = []
    for group in GROUPS:
        steps = len(group)
        cands = jnp.stack(
            [masked[(s % (doc_rows // QUERY)) * QUERY :][:QUERY] for s in group]
        )
        pieces = scatter_from_owner(cands, owners[group[0] : group[-1] + 1], sizes)
        queries = lax.all_gather(pieces, AX, axis=1, tiled=True)
        q_sq = jnp.einsum("sqt,sqt->sq", queries, queries, preferred_element_type=jnp.float32)
        q_inv = lax.rsqrt(lax.psum(q_sq, RP) + EPSILON)
        similar = jnp.einsum("sqt,dt->sqd", queries, masked, preferred_element_type=jnp.float32)
        similar = similar.reshape(steps, n_shard, 2, 2, row_share, doc_rows).transpose(0, 2, 3, 1, 4, 5)
        similar = jnp.sum(exchange(similar, "c", 2), axis=2)
        mine = jnp.sum(exchange(similar, "zl", 1), axis=1)
        my_inv = lax.dynamic_index_in_dim(
            q_inv.reshape(steps, n_shard, n_rep, row_share), rep_index, 2, keepdims=False
        )
        scaled = mine * my_inv[..., None] * inverse[None, None, None, :] * sharpen
        scores = jnp.clip(scaled, -CLIP_LEVEL, CLIP_LEVEL).astype(jnp.bfloat16)
        got = exchange(scores, AX, 1)
        outs.append(got.transpose(0, 2, 1, 3).reshape(steps, row_share, n_shard * doc_rows))
    return jnp.concatenate(outs, axis=0)


def solution(mesh):
    names = dict(zip(("x", "z_hi", "y"), (4, 4, 4)))
    n_shard, n_rep = mesh.devices.shape
    sizes = (names["x"], names["z_hi"], names["y"])
    assert sizes[0] * sizes[1] * sizes[2] == n_shard and n_rep == 4
    mesh5 = Mesh(mesh.devices.reshape(*sizes, 2, 2), AX + RP)
    return jax.shard_map(
        lambda d, p, o: on_device(d, p, o, sizes),
        mesh=mesh5,
        in_specs=(P(AX, RP), P(AX, RP), P()),
        out_specs=P(None, AX + RP, None),
        check_vma=False,
    )
```

```python
import math

import jax
import jax.numpy as jnp
from jax import lax
from jax.sharding import Mesh
from jax.sharding import PartitionSpec as P

TERMS = 16384
QUERY = 256
STEPS = 4


EPSILON = 1e-06
CLIP_LEVEL = 1.5

AX = ("x", "zh", "y")
RP = ("zl", "c")
GROUPS = ((0, 1), (2, 3))


def exchange(buf, name, dim):
    return lax.all_to_all(buf, name, split_axis=dim, concat_axis=dim, tiled=True)


def scatter_from_owner(cand, owners, sizes):
    steps, rows, terms = cand.shape
    nx, nz, ny = sizes
    piece = rows // (nx * nz * ny)
    plane = owners // (nz * ny) * ny + owners % ny
    height = (owners // ny) % nz
    buf = cand.reshape(steps, nx, nz, ny, piece, terms).transpose(0, 1, 3, 2, 4, 5)
    buf = exchange(buf.reshape(steps, nx * ny, nz, piece, terms), ("x", "y"), 1)
    buf = jnp.stack([lax.dynamic_index_in_dim(buf[s], plane[s], 0, keepdims=False) for s in range(steps)])
    buf = exchange(buf, "zh", 1)
    return jnp.stack([lax.dynamic_index_in_dim(buf[s], height[s], 0, keepdims=False) for s in range(steps)])


def on_device(docs, pattern, owners, sizes):
    nx, nz, ny = sizes
    n_shard = nx * nz * ny
    n_rep = lax.axis_size(RP)
    rep_index = lax.axis_index(RP)
    doc_rows, term_cols = docs.shape
    tile_edge = 128
    weights = pattern.astype(jnp.bfloat16)
    masked = (
        docs.reshape(doc_rows // tile_edge, tile_edge, term_cols // tile_edge, tile_edge)
        * weights[:, None, :, None]
    ).reshape(doc_rows, term_cols)
    partial_sq = jnp.einsum("dt,dt->d", masked, masked, preferred_element_type=jnp.float32)
    doc_sq = lax.psum(partial_sq, RP)
    inverse = lax.rsqrt(doc_sq + EPSILON)
    sharpen = math.sqrt(TERMS) * 0.5
    row_share = QUERY // (n_shard * n_rep)
    cands = jnp.stack(
        [masked[(s % (doc_rows // QUERY)) * QUERY :][:QUERY] for s in range(STEPS)]
    )
    pieces = scatter_from_owner(cands, owners, sizes)
    outs = []
    before = None
    for group in GROUPS:
        steps = len(group)
        mine_pieces = pieces[group[0] : group[-1] + 1]
        if before is not None:
            mine_pieces, _ = lax.optimization_barrier((mine_pieces, before))
        queries = lax.all_gather(mine_pieces, AX, axis=1, tiled=True)
        before = queries
        q_sq = jnp.einsum("sqt,sqt->sq", queries, queries, preferred_element_type=jnp.float32)
        q_inv = lax.rsqrt(lax.psum(q_sq, RP) + EPSILON)
        similar = jnp.einsum("sqt,dt->sqd", queries, masked, preferred_element_type=jnp.float32)
        similar = similar.reshape(steps, n_shard, 2, 2, row_share, doc_rows).transpose(0, 2, 3, 1, 4, 5)
        similar = jnp.sum(exchange(similar, "c", 2), axis=2)
        mine = jnp.sum(exchange(similar, "zl", 1), axis=1)
        my_inv = lax.dynamic_index_in_dim(
            q_inv.reshape(steps, n_shard, n_rep, row_share), rep_index, 2, keepdims=False
        )
        scaled = mine * my_inv[..., None] * inverse[None, None, None, :] * sharpen
        scores = jnp.clip(scaled, -CLIP_LEVEL, CLIP_LEVEL).astype(jnp.bfloat16)
        got = exchange(scores, AX, 1)
        outs.append(got.transpose(0, 2, 1, 3).reshape(steps, row_share, n_shard * doc_rows))
    return jnp.concatenate(outs, axis=0)


def solution(mesh):
    names = dict(zip(("x", "z_hi", "y"), (4, 4, 4)))
    n_shard, n_rep = mesh.devices.shape
    sizes = (names["x"], names["z_hi"], names["y"])
    assert sizes[0] * sizes[1] * sizes[2] == n_shard and n_rep == 4
    mesh5 = Mesh(mesh.devices.reshape(*sizes, 2, 2), AX + RP)
    return jax.shard_map(
        lambda d, p, o: on_device(d, p, o, sizes),
        mesh=mesh5,
        in_specs=(P(AX, RP), P(AX, RP), P()),
        out_specs=P(None, AX + RP, None),
        check_vma=False,
    )
```

```python
import math

import jax
import jax.numpy as jnp
from jax import lax
from jax.sharding import Mesh
from jax.sharding import PartitionSpec as P

TERMS = 16384
QUERY = 256
STEPS = 4


EPSILON = 1e-06
CLIP_LEVEL = 1.5

AX = ("x", "zh", "y")
RP = ("zl", "c")


def exchange(buf, name, dim):
    return lax.all_to_all(buf, name, split_axis=dim, concat_axis=dim, tiled=True)


def scatter_from_owner(cands, owners, sizes):
    rows, terms = cands[0].shape
    nx, nz, ny = sizes
    coord = {"x": owners // (nz * ny), "zh": (owners // ny) % nz, "y": owners % ny}
    bufs = [c.reshape(nx, nz, ny, rows // (nx * nz * ny), terms) for c in cands]
    dim = AX.index("y")
    buf = jnp.stack(
        [
            lax.dynamic_slice_in_dim(exchange(b, "y", dim), coord["y"][s], 1, axis=dim)
            for s, b in enumerate(bufs)
        ]
    )
    for name in ("x", "zh"):
        dim = 1 + AX.index(name)
        got = exchange(buf, name, dim)
        buf = jnp.stack(
            [lax.dynamic_slice_in_dim(got[s], coord[name][s], 1, axis=dim - 1) for s in range(len(cands))]
        )
    return buf.reshape(len(cands), rows // (nx * nz * ny), terms)


def on_device(docs, pattern, owners, sizes):
    nx, nz, ny = sizes
    n_shard = nx * nz * ny
    n_rep = lax.axis_size(RP)
    rep_index = lax.axis_index(RP)
    doc_rows, term_cols = docs.shape
    tile_edge = 128
    weights = pattern.astype(jnp.bfloat16)
    masked = (
        docs.reshape(doc_rows // tile_edge, tile_edge, term_cols // tile_edge, tile_edge)
        * weights[:, None, :, None]
    ).reshape(doc_rows, term_cols)
    partial_sq = jnp.einsum("dt,dt->d", masked, masked, preferred_element_type=jnp.float32)
    doc_sq = lax.psum(partial_sq, RP)
    inverse = lax.rsqrt(doc_sq + EPSILON)
    sharpen = math.sqrt(TERMS) * 0.5
    cands = [masked[(s % (doc_rows // QUERY)) * QUERY :][:QUERY] for s in range(STEPS)]
    pieces = scatter_from_owner(cands, owners, sizes)
    queries = lax.all_gather(pieces, AX, axis=1, tiled=True)
    q_sq = jnp.einsum("sqt,sqt->sq", queries, queries, preferred_element_type=jnp.float32)
    q_inv = lax.rsqrt(lax.psum(q_sq, RP) + EPSILON)
    similar = jnp.einsum("sqt,dt->sqd", queries, masked, preferred_element_type=jnp.float32)
    row_share = QUERY // (n_shard * n_rep)
    similar = similar.reshape(STEPS, n_shard, 2, 2, row_share, doc_rows).transpose(0, 2, 3, 1, 4, 5)
    similar = jnp.sum(exchange(similar, "c", 2), axis=2)
    mine = jnp.sum(exchange(similar, "zl", 1), axis=1)
    my_inv = lax.dynamic_index_in_dim(
        q_inv.reshape(STEPS, n_shard, n_rep, row_share), rep_index, 2, keepdims=False
    )
    scaled = mine * my_inv[..., None] * inverse[None, None, None, :] * sharpen
    scores = jnp.clip(scaled, -CLIP_LEVEL, CLIP_LEVEL).astype(jnp.bfloat16)
    got = lax.all_to_all(scores, AX, split_axis=1, concat_axis=1, tiled=True)
    return got.transpose(0, 2, 1, 3).reshape(STEPS, row_share, n_shard * doc_rows)


def solution(mesh):
    names = dict(zip(("x", "z_hi", "y"), (4, 4, 4)))
    n_shard, n_rep = mesh.devices.shape
    sizes = (names["x"], names["z_hi"], names["y"])
    assert sizes[0] * sizes[1] * sizes[2] == n_shard and n_rep == 4
    mesh5 = Mesh(mesh.devices.reshape(*sizes, 2, 2), AX + RP)
    return jax.shard_map(
        lambda d, p, o: on_device(d, p, o, sizes),
        mesh=mesh5,
        in_specs=(P(AX, RP), P(AX, RP), P()),
        out_specs=P(None, AX + RP, None),
        check_vma=False,
    )
```

```python
import math

import jax
import jax.numpy as jnp
from jax import lax
from jax.sharding import Mesh
from jax.sharding import PartitionSpec as P

TERMS = 16384
QUERY = 256
STEPS = 4


EPSILON = 1e-06
CLIP_LEVEL = 1.5

AX = ("x", "zh", "y")
RP = ("zl", "c")


def exchange(buf, name, dim):
    return lax.all_to_all(buf, name, split_axis=dim, concat_axis=dim, tiled=True)


def scatter_from_owner(cands, owners, sizes):
    rows, terms = cands[0].shape
    nx, nz, ny = sizes
    coord = {"x": owners // (nz * ny), "zh": (owners // ny) % nz, "y": owners % ny}
    bufs = [c.reshape(nx, nz, ny, rows // (nx * nz * ny), terms) for c in cands]
    dim = AX.index("y")
    buf = jnp.stack(
        [
            lax.dynamic_slice_in_dim(exchange(b, "y", dim), coord["y"][s], 1, axis=dim)
            for s, b in enumerate(bufs)
        ]
    )
    for name in ("x", "zh"):
        dim = 1 + AX.index(name)
        got = exchange(buf, name, dim)
        buf = jnp.stack(
            [lax.dynamic_slice_in_dim(got[s], coord[name][s], 1, axis=dim - 1) for s in range(len(cands))]
        )
    return buf.reshape(len(cands), rows // (nx * nz * ny), terms)


def on_device(docs, pattern, owners, sizes):
    nx, nz, ny = sizes
    n_shard = nx * nz * ny
    n_rep = lax.axis_size(RP)
    rep_index = lax.axis_index(RP)
    doc_rows, term_cols = docs.shape
    tile_edge = 128
    weights = pattern.astype(jnp.bfloat16)
    masked = (
        docs.reshape(doc_rows // tile_edge, tile_edge, term_cols // tile_edge, tile_edge)
        * weights[:, None, :, None]
    ).reshape(doc_rows, term_cols)
    partial_sq = jnp.einsum("dt,dt->d", masked, masked, preferred_element_type=jnp.float32)
    doc_sq = lax.psum(partial_sq, RP)
    inverse = lax.rsqrt(doc_sq + EPSILON)
    sharpen = math.sqrt(TERMS) * 0.5
    cands = [masked[(s % (doc_rows // QUERY)) * QUERY :][:QUERY] for s in range(STEPS)]
    pieces = scatter_from_owner(cands, owners, sizes)
    queries = lax.all_gather(pieces, AX, axis=1, tiled=True)
    q_sq = jnp.einsum("sqt,sqt->sq", queries, queries, preferred_element_type=jnp.float32)
    q_inv = lax.rsqrt(lax.psum(q_sq, RP) + EPSILON)
    flat_queries, stored = lax.optimization_barrier((queries.reshape(STEPS * QUERY, term_cols), masked))
    similar = lax.optimization_barrier(
        lax.dot_general(flat_queries, stored, (((1,), (1,)), ((), ())), preferred_element_type=jnp.float32)
    )
    row_share = QUERY // (n_shard * n_rep)
    similar = similar.reshape(STEPS, n_shard, 2, 2, row_share, doc_rows).transpose(0, 2, 3, 1, 4, 5)
    similar = jnp.sum(exchange(similar, "c", 2), axis=2)
    mine = jnp.sum(exchange(similar, "zl", 1), axis=1)
    my_inv = lax.dynamic_index_in_dim(
        q_inv.reshape(STEPS, n_shard, n_rep, row_share), rep_index, 2, keepdims=False
    )
    scaled = mine * my_inv[..., None] * inverse[None, None, None, :] * sharpen
    scores = jnp.clip(scaled, -CLIP_LEVEL, CLIP_LEVEL).astype(jnp.bfloat16)
    got = lax.all_to_all(scores, AX, split_axis=1, concat_axis=1, tiled=True)
    return got.transpose(0, 2, 1, 3).reshape(STEPS, row_share, n_shard * doc_rows)


def solution(mesh):
    names = dict(zip(("x", "z_hi", "y"), (4, 4, 4)))
    n_shard, n_rep = mesh.devices.shape
    sizes = (names["x"], names["z_hi"], names["y"])
    assert sizes[0] * sizes[1] * sizes[2] == n_shard and n_rep == 4
    mesh5 = Mesh(mesh.devices.reshape(*sizes, 2, 2), AX + RP)
    return jax.shard_map(
        lambda d, p, o: on_device(d, p, o, sizes),
        mesh=mesh5,
        in_specs=(P(AX, RP), P(AX, RP), P()),
        out_specs=P(None, AX + RP, None),
        check_vma=False,
    )
```

```python
import math

import jax
import jax.numpy as jnp
from jax import lax
from jax.sharding import Mesh
from jax.sharding import PartitionSpec as P

TERMS = 16384
QUERY = 256
STEPS = 4


EPSILON = 1e-06
CLIP_LEVEL = 1.5

AX = ("x", "zh", "y")
RP = ("zl", "c")


def exchange(buf, name, dim):
    return lax.all_to_all(buf, name, split_axis=dim, concat_axis=dim, tiled=True)


def scatter_from_owner(cands, owners, sizes):
    rows, terms = cands[0].shape
    nx, nz, ny = sizes
    coord = {"x": owners // (nz * ny), "zh": (owners // ny) % nz, "y": owners % ny}
    bufs = [c.reshape(nx, nz, ny, rows // (nx * nz * ny), terms) for c in cands]
    dim = AX.index("y")
    buf = jnp.stack(
        [
            lax.dynamic_slice_in_dim(exchange(b, "y", dim), coord["y"][s], 1, axis=dim)
            for s, b in enumerate(bufs)
        ]
    )
    for name in ("x", "zh"):
        dim = 1 + AX.index(name)
        got = exchange(buf, name, dim)
        buf = jnp.stack(
            [lax.dynamic_slice_in_dim(got[s], coord[name][s], 1, axis=dim - 1) for s in range(len(cands))]
        )
    return buf.reshape(len(cands), rows // (nx * nz * ny), terms)


def on_device(docs, pattern, owners, sizes):
    nx, nz, ny = sizes
    n_shard = nx * nz * ny
    n_rep = lax.axis_size(RP)
    rep_index = lax.axis_index(RP)
    doc_rows, term_cols = docs.shape
    tile_edge = 128
    weights = pattern.astype(jnp.bfloat16)
    masked = (
        docs.reshape(doc_rows // tile_edge, tile_edge, term_cols // tile_edge, tile_edge)
        * weights[:, None, :, None]
    ).reshape(doc_rows, term_cols)
    partial_sq = jnp.einsum("dt,dt->d", masked, masked, preferred_element_type=jnp.float32)
    doc_sq = lax.psum(partial_sq, RP)
    inverse = lax.rsqrt(doc_sq + EPSILON)
    sharpen = math.sqrt(TERMS) * 0.5
    cands = [masked[(s % (doc_rows // QUERY)) * QUERY :][:QUERY] for s in range(STEPS)]
    pieces = scatter_from_owner(cands, owners, sizes)
    piece = pieces.shape[1]
    flat_queries = lax.all_gather(pieces.reshape(STEPS * piece, term_cols), AX, axis=0, tiled=True)
    q_sq = jnp.einsum("qt,qt->q", flat_queries, flat_queries, preferred_element_type=jnp.float32)
    q_inv = lax.rsqrt(lax.psum(q_sq, RP) + EPSILON).reshape(n_shard, STEPS, piece)
    flat_queries, stored = lax.optimization_barrier((flat_queries, masked))
    similar = lax.optimization_barrier(
        lax.dot_general(flat_queries, stored, (((1,), (1,)), ((), ())), preferred_element_type=jnp.float32)
    )
    row_share = piece // n_rep
    similar = similar.reshape(n_shard, STEPS, 2, 2, row_share, doc_rows)
    similar = jnp.sum(exchange(similar, "c", 3), axis=3)
    mine = jnp.sum(exchange(similar, "zl", 2), axis=2)
    my_inv = lax.dynamic_slice_in_dim(q_inv, rep_index * row_share, row_share, axis=2)
    scaled = mine * my_inv[..., None] * inverse[None, None, None, :] * sharpen
    scores = jnp.clip(scaled, -CLIP_LEVEL, CLIP_LEVEL).astype(jnp.bfloat16)
    got = exchange(scores, AX, 0)
    return got.transpose(1, 2, 0, 3).reshape(STEPS, row_share, n_shard * doc_rows)


def solution(mesh):
    names = dict(zip(("x", "z_hi", "y"), (4, 4, 4)))
    n_shard, n_rep = mesh.devices.shape
    sizes = (names["x"], names["z_hi"], names["y"])
    assert sizes[0] * sizes[1] * sizes[2] == n_shard and n_rep == 4
    mesh5 = Mesh(mesh.devices.reshape(*sizes, 2, 2), AX + RP)
    return jax.shard_map(
        lambda d, p, o: on_device(d, p, o, sizes),
        mesh=mesh5,
        in_specs=(P(AX, RP), P(AX, RP), P()),
        out_specs=P(None, AX + RP, None),
        check_vma=False,
    )
```

```python
import math

import jax
import jax.numpy as jnp
from jax import lax
from jax.sharding import Mesh
from jax.sharding import PartitionSpec as P

TERMS = 16384
QUERY = 256
STEPS = 4


EPSILON = 1e-06
CLIP_LEVEL = 1.5

AX = ("x", "zh", "y")
RP = ("zl", "c")


def exchange(buf, name, dim):
    return lax.all_to_all(buf, name, split_axis=dim, concat_axis=dim, tiled=True)


def scatter_from_owner(blocks, block_of, owners, sizes):
    rows, terms = blocks[0].shape
    nx, nz, ny = sizes
    steps = len(block_of)
    coord = {"x": owners // (nz * ny), "zh": (owners // ny) % nz, "y": owners % ny}
    dim = AX.index("y")
    got = [exchange(blk.reshape(nx, nz, ny, rows // (nx * nz * ny), terms), "y", dim) for blk in blocks]
    buf = jnp.stack(
        [lax.dynamic_slice_in_dim(got[block_of[s]], coord["y"][s], 1, axis=dim) for s in range(steps)]
    )
    for name in ("x", "zh"):
        dim = 1 + AX.index(name)
        got = exchange(buf, name, dim)
        buf = jnp.stack(
            [lax.dynamic_slice_in_dim(got[s], coord[name][s], 1, axis=dim - 1) for s in range(steps)]
        )
    return buf.reshape(steps, rows // (nx * nz * ny), terms)


def on_device(docs, pattern, owners, sizes):
    nx, nz, ny = sizes
    n_shard = nx * nz * ny
    n_rep = lax.axis_size(RP)
    rep_index = lax.axis_index(RP)
    doc_rows, term_cols = docs.shape
    tile_edge = 128
    weights = pattern.astype(jnp.bfloat16)
    masked = (
        docs.reshape(doc_rows // tile_edge, tile_edge, term_cols // tile_edge, tile_edge)
        * weights[:, None, :, None]
    ).reshape(doc_rows, term_cols)
    partial_sq = jnp.einsum("dt,dt->d", masked, masked, preferred_element_type=jnp.float32)
    doc_sq = lax.psum(partial_sq, RP)
    inverse = lax.rsqrt(doc_sq + EPSILON)
    sharpen = math.sqrt(TERMS) * 0.5
    blocks = [masked[k * QUERY :][:QUERY] for k in range(doc_rows // QUERY)]
    block_of = [s % (doc_rows // QUERY) for s in range(STEPS)]
    pieces = scatter_from_owner(blocks, block_of, owners, sizes)
    piece = pieces.shape[1]
    flat_queries = lax.all_gather(pieces.reshape(STEPS * piece, term_cols), AX, axis=0, tiled=True)
    q_sq = jnp.einsum("qt,qt->q", flat_queries, flat_queries, preferred_element_type=jnp.float32)
    q_inv = lax.rsqrt(lax.psum(q_sq, RP) + EPSILON).reshape(n_shard, STEPS, piece)
    flat_queries, stored = lax.optimization_barrier((flat_queries, masked))
    similar = lax.optimization_barrier(
        lax.dot_general(flat_queries, stored, (((1,), (1,)), ((), ())), preferred_element_type=jnp.float32)
    )
    row_share = piece // n_rep
    similar = similar.reshape(n_shard, STEPS, 2, 2, row_share, doc_rows)
    similar = jnp.sum(exchange(similar, "c", 3), axis=3)
    mine = jnp.sum(exchange(similar, "zl", 2), axis=2)
    my_inv = lax.dynamic_slice_in_dim(q_inv, rep_index * row_share, row_share, axis=2)
    scaled = mine * my_inv[..., None] * inverse[None, None, None, :] * sharpen
    scores = jnp.clip(scaled, -CLIP_LEVEL, CLIP_LEVEL).astype(jnp.bfloat16)
    got = exchange(scores, AX, 0)
    return got.transpose(1, 2, 0, 3).reshape(STEPS, row_share, n_shard * doc_rows)


def solution(mesh):
    names = dict(zip(("x", "z_hi", "y"), (4, 4, 4)))
    n_shard, n_rep = mesh.devices.shape
    sizes = (names["x"], names["z_hi"], names["y"])
    assert sizes[0] * sizes[1] * sizes[2] == n_shard and n_rep == 4
    mesh5 = Mesh(mesh.devices.reshape(*sizes, 2, 2), AX + RP)
    return jax.shard_map(
        lambda d, p, o: on_device(d, p, o, sizes),
        mesh=mesh5,
        in_specs=(P(AX, RP), P(AX, RP), P()),
        out_specs=P(None, AX + RP, None),
        check_vma=False,
    )
```

```python
import math

import jax
import jax.numpy as jnp
from jax import lax
from jax.sharding import Mesh
from jax.sharding import PartitionSpec as P

TERMS = 16384
QUERY = 256
STEPS = 4


EPSILON = 1e-06
CLIP_LEVEL = 1.5

AX = ("x", "zh", "y")
RP = ("zl", "c")


def exchange(buf, name, dim):
    return lax.all_to_all(buf, name, split_axis=dim, concat_axis=dim, tiled=True)


def scatter_from_owner(blocks, block_of, owners, sizes):
    rows, terms = blocks[0].shape
    nx, nz, ny = sizes
    steps = len(block_of)
    coord = {"x": owners // (nz * ny), "zh": (owners // ny) % nz, "y": owners % ny}
    dim = AX.index("y")
    got = [exchange(blk.reshape(nx, nz, ny, rows // (nx * nz * ny), terms), "y", dim) for blk in blocks]
    buf = jnp.stack(
        [lax.dynamic_slice_in_dim(got[block_of[s]], coord["y"][s], 1, axis=dim) for s in range(steps)]
    )
    for name in ("x", "zh"):
        dim = 1 + AX.index(name)
        got = exchange(buf, name, dim)
        buf = jnp.stack(
            [lax.dynamic_slice_in_dim(got[s], coord[name][s], 1, axis=dim - 1) for s in range(steps)]
        )
    return buf.reshape(steps, rows // (nx * nz * ny), terms)


def on_device(docs, pattern, owners, sizes):
    nx, nz, ny = sizes
    n_shard = nx * nz * ny
    n_rep = lax.axis_size(RP)
    rep_index = lax.axis_index(RP)
    doc_rows, term_cols = docs.shape
    tile_edge = 128
    weights = pattern.astype(jnp.bfloat16)
    masked = (
        docs.reshape(doc_rows // tile_edge, tile_edge, term_cols // tile_edge, tile_edge)
        * weights[:, None, :, None]
    ).reshape(doc_rows, term_cols)
    partial_sq = jnp.einsum("dt,dt->d", masked, masked, preferred_element_type=jnp.float32)
    sharpen = math.sqrt(TERMS) * 0.5
    blocks = [masked[k * QUERY :][:QUERY] for k in range(doc_rows // QUERY)]
    block_of = [s % (doc_rows // QUERY) for s in range(STEPS)]
    pieces = scatter_from_owner(blocks, block_of, owners, sizes)
    piece = pieces.shape[1]
    flat_queries = lax.all_gather(pieces.reshape(STEPS * piece, term_cols), AX, axis=0, tiled=True)
    q_sq = jnp.einsum("qt,qt->q", flat_queries, flat_queries, preferred_element_type=jnp.float32)
    flat_queries, stored = lax.optimization_barrier((flat_queries, masked))
    similar = lax.optimization_barrier(
        lax.dot_general(flat_queries, stored, (((1,), (1,)), ((), ())), preferred_element_type=jnp.float32)
    )
    row_share = piece // n_rep
    block = (n_shard, STEPS, 2, 2, row_share)
    similar = jnp.concatenate([similar.reshape(*block, doc_rows), q_sq.reshape(*block, 1)], axis=-1)
    doc_row = jnp.broadcast_to(
        jnp.concatenate([partial_sq, jnp.zeros((1,), jnp.float32)]), (1, *block[1:], doc_rows + 1)
    )
    similar = jnp.concatenate([similar, doc_row], axis=0)
    similar = jnp.sum(exchange(similar, "c", 3), axis=3)
    total = jnp.sum(exchange(similar, "zl", 2), axis=2)
    mine = total[:n_shard, :, :, :doc_rows]
    inverse = lax.rsqrt(total[n_shard, 0, 0, :doc_rows] + EPSILON)
    my_inv = lax.rsqrt(total[:n_shard, :, :, doc_rows] + EPSILON)
    scaled = mine * my_inv[..., None] * inverse[None, None, None, :] * sharpen
    scores = jnp.clip(scaled, -CLIP_LEVEL, CLIP_LEVEL).astype(jnp.bfloat16)
    got = exchange(scores, AX, 0)
    return got.transpose(1, 2, 0, 3).reshape(STEPS, row_share, n_shard * doc_rows)


def solution(mesh):
    names = dict(zip(("x", "z_hi", "y"), (4, 4, 4)))
    n_shard, n_rep = mesh.devices.shape
    sizes = (names["x"], names["z_hi"], names["y"])
    assert sizes[0] * sizes[1] * sizes[2] == n_shard and n_rep == 4
    mesh5 = Mesh(mesh.devices.reshape(*sizes, 2, 2), AX + RP)
    return jax.shard_map(
        lambda d, p, o: on_device(d, p, o, sizes),
        mesh=mesh5,
        in_specs=(P(AX, RP), P(AX, RP), P()),
        out_specs=P(None, AX + RP, None),
        check_vma=False,
    )
```

```python
import math

import jax
import jax.numpy as jnp
from jax import lax
from jax.sharding import Mesh
from jax.sharding import PartitionSpec as P

TERMS = 16384
QUERY = 256
STEPS = 4


EPSILON = 1e-06
CLIP_LEVEL = 1.5

AX = ("x", "zh", "y")
RP = ("zl", "c")


def exchange(buf, name, dim):
    return lax.all_to_all(buf, name, split_axis=dim, concat_axis=dim, tiled=True)


def scatter_from_owner(blocks, block_of, owners, sizes):
    rows, terms = blocks[0].shape
    nx, nz, ny = sizes
    steps = len(block_of)
    coord = {"x": owners // (nz * ny), "zh": (owners // ny) % nz, "y": owners % ny}
    dim = AX.index("y")
    got = [exchange(blk.reshape(nx, nz, ny, rows // (nx * nz * ny), terms), "y", dim) for blk in blocks]
    buf = jnp.stack(
        [lax.dynamic_slice_in_dim(got[block_of[s]], coord["y"][s], 1, axis=dim) for s in range(steps)]
    )
    plane = coord["x"] * nz + coord["zh"]
    got = exchange(buf.reshape(steps, nx * nz, rows // (nx * nz * ny), terms), ("x", "zh"), 1)
    return jnp.stack([lax.dynamic_index_in_dim(got[s], plane[s], 0, keepdims=False) for s in range(steps)])


def on_device(docs, pattern, owners, sizes):
    nx, nz, ny = sizes
    n_shard = nx * nz * ny
    n_rep = lax.axis_size(RP)
    rep_index = lax.axis_index(RP)
    doc_rows, term_cols = docs.shape
    tile_edge = 128
    weights = pattern.astype(jnp.bfloat16)
    masked = (
        docs.reshape(doc_rows // tile_edge, tile_edge, term_cols // tile_edge, tile_edge)
        * weights[:, None, :, None]
    ).reshape(doc_rows, term_cols)
    partial_sq = jnp.einsum("dt,dt->d", masked, masked, preferred_element_type=jnp.float32)
    doc_sq = lax.psum(partial_sq, RP)
    inverse = lax.rsqrt(doc_sq + EPSILON)
    sharpen = math.sqrt(TERMS) * 0.5
    blocks = [masked[k * QUERY :][:QUERY] for k in range(doc_rows // QUERY)]
    block_of = [s % (doc_rows // QUERY) for s in range(STEPS)]
    pieces = scatter_from_owner(blocks, block_of, owners, sizes)
    piece = pieces.shape[1]
    flat_queries = lax.all_gather(pieces.reshape(STEPS * piece, term_cols), AX, axis=0, tiled=True)
    q_sq = jnp.einsum("qt,qt->q", flat_queries, flat_queries, preferred_element_type=jnp.float32)
    q_inv = lax.rsqrt(lax.psum(q_sq, RP) + EPSILON).reshape(n_shard, STEPS, piece)
    flat_queries, stored = lax.optimization_barrier((flat_queries, masked))
    similar = lax.optimization_barrier(
        lax.dot_general(flat_queries, stored, (((1,), (1,)), ((), ())), preferred_element_type=jnp.float32)
    )
    row_share = piece // n_rep
    similar = similar.reshape(n_shard, STEPS, 2, 2, row_share, doc_rows)
    similar = jnp.sum(exchange(similar, "c", 3), axis=3)
    mine = jnp.sum(exchange(similar, "zl", 2), axis=2)
    my_inv = lax.dynamic_slice_in_dim(q_inv, rep_index * row_share, row_share, axis=2)
    scaled = mine * my_inv[..., None] * inverse[None, None, None, :] * sharpen
    scores = jnp.clip(scaled, -CLIP_LEVEL, CLIP_LEVEL).astype(jnp.bfloat16)
    got = exchange(scores, AX, 0)
    return got.transpose(1, 2, 0, 3).reshape(STEPS, row_share, n_shard * doc_rows)


def solution(mesh):
    names = dict(zip(("x", "z_hi", "y"), (4, 4, 4)))
    n_shard, n_rep = mesh.devices.shape
    sizes = (names["x"], names["z_hi"], names["y"])
    assert sizes[0] * sizes[1] * sizes[2] == n_shard and n_rep == 4
    mesh5 = Mesh(mesh.devices.reshape(*sizes, 2, 2), AX + RP)
    return jax.shard_map(
        lambda d, p, o: on_device(d, p, o, sizes),
        mesh=mesh5,
        in_specs=(P(AX, RP), P(AX, RP), P()),
        out_specs=P(None, AX + RP, None),
        check_vma=False,
    )
```

```python
import math

import jax
import jax.numpy as jnp
from jax import lax
from jax.sharding import Mesh
from jax.sharding import PartitionSpec as P

TERMS = 16384
QUERY = 256
STEPS = 4


EPSILON = 1e-06
CLIP_LEVEL = 1.5

AX = ("x", "zh", "y")
RP = ("zl", "c")


def exchange(buf, name, dim):
    return lax.all_to_all(buf, name, split_axis=dim, concat_axis=dim, tiled=True)


def scatter_from_owner(blocks, block_of, owners, sizes):
    rows, terms = blocks[0].shape
    nx, nz, ny = sizes
    steps = len(block_of)
    coord = {"x": owners // (nz * ny), "zh": (owners // ny) % nz, "y": owners % ny}
    dim = AX.index("y")
    stacked = jnp.stack(blocks).reshape(len(blocks), nx, nz, ny, rows // (nx * nz * ny), terms)
    got = exchange(stacked, "y", 1 + dim)
    buf = jnp.stack(
        [lax.dynamic_slice_in_dim(got[block_of[s]], coord["y"][s], 1, axis=dim) for s in range(steps)]
    )
    for name in ("x", "zh"):
        dim = 1 + AX.index(name)
        got = exchange(buf, name, dim)
        buf = jnp.stack(
            [lax.dynamic_slice_in_dim(got[s], coord[name][s], 1, axis=dim - 1) for s in range(steps)]
        )
    return buf.reshape(steps, rows // (nx * nz * ny), terms)


def on_device(docs, pattern, owners, sizes):
    nx, nz, ny = sizes
    n_shard = nx * nz * ny
    n_rep = lax.axis_size(RP)
    rep_index = lax.axis_index(RP)
    doc_rows, term_cols = docs.shape
    tile_edge = 128
    weights = pattern.astype(jnp.bfloat16)
    masked = (
        docs.reshape(doc_rows // tile_edge, tile_edge, term_cols // tile_edge, tile_edge)
        * weights[:, None, :, None]
    ).reshape(doc_rows, term_cols)
    partial_sq = jnp.einsum("dt,dt->d", masked, masked, preferred_element_type=jnp.float32)
    doc_sq = lax.psum(partial_sq, RP)
    inverse = lax.rsqrt(doc_sq + EPSILON)
    sharpen = math.sqrt(TERMS) * 0.5
    blocks = [masked[k * QUERY :][:QUERY] for k in range(doc_rows // QUERY)]
    block_of = [s % (doc_rows // QUERY) for s in range(STEPS)]
    pieces = scatter_from_owner(blocks, block_of, owners, sizes)
    piece = pieces.shape[1]
    flat_queries = lax.all_gather(pieces.reshape(STEPS * piece, term_cols), AX, axis=0, tiled=True)
    q_sq = jnp.einsum("qt,qt->q", flat_queries, flat_queries, preferred_element_type=jnp.float32)
    q_inv = lax.rsqrt(lax.psum(q_sq, RP) + EPSILON).reshape(n_shard, STEPS, piece)
    flat_queries, stored = lax.optimization_barrier((flat_queries, masked))
    similar = lax.optimization_barrier(
        lax.dot_general(flat_queries, stored, (((1,), (1,)), ((), ())), preferred_element_type=jnp.float32)
    )
    row_share = piece // n_rep
    similar = similar.reshape(n_shard, STEPS, 2, 2, row_share, doc_rows)
    similar = jnp.sum(exchange(similar, "c", 3), axis=3)
    mine = jnp.sum(exchange(similar, "zl", 2), axis=2)
    my_inv = lax.dynamic_slice_in_dim(q_inv, rep_index * row_share, row_share, axis=2)
    scaled = mine * my_inv[..., None] * inverse[None, None, None, :] * sharpen
    scores = jnp.clip(scaled, -CLIP_LEVEL, CLIP_LEVEL).astype(jnp.bfloat16)
    got = exchange(scores, AX, 0)
    return got.transpose(1, 2, 0, 3).reshape(STEPS, row_share, n_shard * doc_rows)


def solution(mesh):
    names = dict(zip(("x", "z_hi", "y"), (4, 4, 4)))
    n_shard, n_rep = mesh.devices.shape
    sizes = (names["x"], names["z_hi"], names["y"])
    assert sizes[0] * sizes[1] * sizes[2] == n_shard and n_rep == 4
    mesh5 = Mesh(mesh.devices.reshape(*sizes, 2, 2), AX + RP)
    return jax.shard_map(
        lambda d, p, o: on_device(d, p, o, sizes),
        mesh=mesh5,
        in_specs=(P(AX, RP), P(AX, RP), P()),
        out_specs=P(None, AX + RP, None),
        check_vma=False,
    )
```

```python
import math

import jax
import jax.numpy as jnp
from jax import lax
from jax.sharding import Mesh
from jax.sharding import PartitionSpec as P

TERMS = 16384
QUERY = 256
STEPS = 4


EPSILON = 1e-06
CLIP_LEVEL = 1.5

AX = ("x", "zh", "y")
RP = ("zl", "c")


def exchange(buf, name, dim):
    return lax.all_to_all(buf, name, split_axis=dim, concat_axis=dim, tiled=True)


def scatter_from_owner(blocks, block_of, owners, sizes):
    rows, terms = blocks[0].shape
    nx, nz, ny = sizes
    steps = len(block_of)
    coord = {"x": owners // (nz * ny), "zh": (owners // ny) % nz, "y": owners % ny}
    dim = AX.index("y")
    got = [exchange(blk.reshape(nx, nz, ny, rows // (nx * nz * ny), terms), "y", dim) for blk in blocks]
    buf = jnp.stack(
        [lax.dynamic_slice_in_dim(got[block_of[s]], coord["y"][s], 1, axis=dim) for s in range(steps)]
    )
    for name in ("x", "zh"):
        dim = 1 + AX.index(name)
        got = exchange(buf, name, dim)
        buf = jnp.stack(
            [lax.dynamic_slice_in_dim(got[s], coord[name][s], 1, axis=dim - 1) for s in range(steps)]
        )
    return buf.reshape(steps, rows // (nx * nz * ny), terms)


def on_device(docs, pattern, owners, sizes):
    nx, nz, ny = sizes
    n_shard = nx * nz * ny
    n_rep = lax.axis_size(RP)
    rep_index = lax.axis_index(RP)
    doc_rows, term_cols = docs.shape
    tile_edge = 128
    weights = pattern.astype(jnp.bfloat16)
    masked = (
        docs.reshape(doc_rows // tile_edge, tile_edge, term_cols // tile_edge, tile_edge)
        * weights[:, None, :, None]
    ).reshape(doc_rows, term_cols)
    partial_sq = jnp.einsum("dt,dt->d", masked, masked, preferred_element_type=jnp.float32)
    doc_sq = lax.psum(partial_sq, RP)
    inverse = lax.rsqrt(doc_sq + EPSILON)
    sharpen = math.sqrt(TERMS) * 0.5
    blocks = [masked[k * QUERY :][:QUERY] for k in range(doc_rows // QUERY)]
    block_of = [s % (doc_rows // QUERY) for s in range(STEPS)]
    pieces = scatter_from_owner(blocks, block_of, owners, sizes)
    piece = pieces.shape[1]
    flat_queries = lax.all_gather(pieces.reshape(STEPS * piece, term_cols), AX, axis=0, tiled=True)
    q_sq = jnp.einsum("qt,qt->q", flat_queries, flat_queries, preferred_element_type=jnp.float32)
    q_sq, inverse = lax.optimization_barrier((q_sq, inverse))
    q_inv = lax.rsqrt(lax.psum(q_sq, RP) + EPSILON).reshape(n_shard, STEPS, piece)
    flat_queries, stored = lax.optimization_barrier((flat_queries, masked))
    similar = lax.optimization_barrier(
        lax.dot_general(flat_queries, stored, (((1,), (1,)), ((), ())), preferred_element_type=jnp.float32)
    )
    row_share = piece // n_rep
    similar = similar.reshape(n_shard, STEPS, 2, 2, row_share, doc_rows)
    similar = jnp.sum(exchange(similar, "c", 3), axis=3)
    mine = jnp.sum(exchange(similar, "zl", 2), axis=2)
    my_inv = lax.dynamic_slice_in_dim(q_inv, rep_index * row_share, row_share, axis=2)
    scaled = mine * my_inv[..., None] * inverse[None, None, None, :] * sharpen
    scores = jnp.clip(scaled, -CLIP_LEVEL, CLIP_LEVEL).astype(jnp.bfloat16)
    got = exchange(scores, AX, 0)
    return got.transpose(1, 2, 0, 3).reshape(STEPS, row_share, n_shard * doc_rows)


def solution(mesh):
    names = dict(zip(("x", "z_hi", "y"), (4, 4, 4)))
    n_shard, n_rep = mesh.devices.shape
    sizes = (names["x"], names["z_hi"], names["y"])
    assert sizes[0] * sizes[1] * sizes[2] == n_shard and n_rep == 4
    mesh5 = Mesh(mesh.devices.reshape(*sizes, 2, 2), AX + RP)
    return jax.shard_map(
        lambda d, p, o: on_device(d, p, o, sizes),
        mesh=mesh5,
        in_specs=(P(AX, RP), P(AX, RP), P()),
        out_specs=P(None, AX + RP, None),
        check_vma=False,
    )
```

```python
import math

import jax
import jax.numpy as jnp
from jax import lax
from jax.sharding import Mesh
from jax.sharding import PartitionSpec as P

TERMS = 16384
QUERY = 256
STEPS = 4


EPSILON = 1e-06
CLIP_LEVEL = 1.5

AX = ("x", "zh", "y")
RP = ("zl", "c")


def exchange(buf, name, dim):
    return lax.all_to_all(buf, name, split_axis=dim, concat_axis=dim, tiled=True)


def scatter_from_owner(blocks, block_of, owners, sizes):
    rows, terms = blocks[0].shape
    nx, nz, ny = sizes
    steps = len(block_of)
    coord = {"x": owners // (nz * ny), "zh": (owners // ny) % nz, "y": owners % ny}
    dim = AX.index("y")
    got = [exchange(blk.reshape(nx, nz, ny, rows // (nx * nz * ny), terms), "y", dim) for blk in blocks]
    buf = jnp.stack(
        [lax.dynamic_slice_in_dim(got[block_of[s]], coord["y"][s], 1, axis=dim) for s in range(steps)]
    )
    for name in ("x", "zh"):
        dim = 1 + AX.index(name)
        got = exchange(buf, name, dim)
        buf = jnp.stack(
            [lax.dynamic_slice_in_dim(got[s], coord[name][s], 1, axis=dim - 1) for s in range(steps)]
        )
    return buf.reshape(steps, rows // (nx * nz * ny), terms)


def on_device(docs, pattern, owners, sizes):
    nx, nz, ny = sizes
    n_shard = nx * nz * ny
    n_rep = lax.axis_size(RP)
    rep_index = lax.axis_index(RP)
    doc_rows, term_cols = docs.shape
    tile_edge = 128
    weights = pattern.astype(jnp.bfloat16)
    masked = (
        docs.reshape(doc_rows // tile_edge, tile_edge, term_cols // tile_edge, tile_edge)
        * weights[:, None, :, None]
    ).reshape(doc_rows, term_cols)
    partial_sq = jnp.einsum("dt,dt->d", masked, masked, preferred_element_type=jnp.float32)
    doc_sq = lax.psum(partial_sq, RP)
    inverse = lax.rsqrt(doc_sq + EPSILON)
    sharpen = math.sqrt(TERMS) * 0.5
    blocks = [masked[k * QUERY :][:QUERY] for k in range(doc_rows // QUERY)]
    block_of = [s % (doc_rows // QUERY) for s in range(STEPS)]
    pieces = scatter_from_owner(blocks, block_of, owners, sizes)
    piece = pieces.shape[1]
    row_share = piece // n_rep
    own_sq = lax.psum(jnp.einsum("spt,spt->sp", pieces, pieces, preferred_element_type=jnp.float32), RP)
    own_inv = lax.dynamic_slice_in_dim(lax.rsqrt(own_sq + EPSILON), rep_index * row_share, row_share, axis=1)
    flat_queries = lax.all_gather(pieces.reshape(STEPS * piece, term_cols), AX, axis=0, tiled=True)
    flat_queries, stored = lax.optimization_barrier((flat_queries, masked))
    similar = lax.optimization_barrier(
        lax.dot_general(flat_queries, stored, (((1,), (1,)), ((), ())), preferred_element_type=jnp.float32)
    )
    similar = similar.reshape(n_shard, STEPS, 2, 2, row_share, doc_rows)
    similar = jnp.sum(exchange(similar, "c", 3), axis=3)
    mine = jnp.sum(exchange(similar, "zl", 2), axis=2)
    weighted = mine * inverse[None, None, None, :]
    got = exchange(weighted, AX, 0)
    scaled = got * own_inv[None, :, :, None] * sharpen
    scores = jnp.clip(scaled, -CLIP_LEVEL, CLIP_LEVEL).astype(jnp.bfloat16)
    return scores.transpose(1, 2, 0, 3).reshape(STEPS, row_share, n_shard * doc_rows)


def solution(mesh):
    names = dict(zip(("x", "z_hi", "y"), (4, 4, 4)))
    n_shard, n_rep = mesh.devices.shape
    sizes = (names["x"], names["z_hi"], names["y"])
    assert sizes[0] * sizes[1] * sizes[2] == n_shard and n_rep == 4
    mesh5 = Mesh(mesh.devices.reshape(*sizes, 2, 2), AX + RP)
    return jax.shard_map(
        lambda d, p, o: on_device(d, p, o, sizes),
        mesh=mesh5,
        in_specs=(P(AX, RP), P(AX, RP), P()),
        out_specs=P(None, AX + RP, None),
        check_vma=False,
    )
```

```python
import math

import jax
import jax.numpy as jnp
from jax import lax
from jax.sharding import Mesh
from jax.sharding import PartitionSpec as P

TERMS = 16384
QUERY = 256
STEPS = 4


EPSILON = 1e-06
CLIP_LEVEL = 1.5

AX = ("x", "zh", "y")
RP = ("zl", "c")


def exchange(buf, name, dim):
    return lax.all_to_all(buf, name, split_axis=dim, concat_axis=dim, tiled=True)


def scatter_from_owner(blocks, block_of, owners, sizes):
    rows, terms = blocks[0].shape
    nx, nz, ny = sizes
    steps = len(block_of)
    coord = {"x": owners // (nz * ny), "zh": (owners // ny) % nz, "y": owners % ny}
    dim = AX.index("y")
    got = [exchange(blk.reshape(nx, nz, ny, rows // (nx * nz * ny), terms), "y", dim) for blk in blocks]
    buf = jnp.stack(
        [lax.dynamic_slice_in_dim(got[block_of[s]], coord["y"][s], 1, axis=dim) for s in range(steps)]
    )
    for name in ("x", "zh"):
        dim = 1 + AX.index(name)
        got = exchange(buf, name, dim)
        buf = jnp.stack(
            [lax.dynamic_slice_in_dim(got[s], coord[name][s], 1, axis=dim - 1) for s in range(steps)]
        )
    return buf.reshape(steps, rows // (nx * nz * ny), terms)


def on_device(docs, pattern, owners, sizes):
    nx, nz, ny = sizes
    n_shard = nx * nz * ny
    n_rep = lax.axis_size(RP)
    rep_index = lax.axis_index(RP)
    doc_rows, term_cols = docs.shape
    tile_edge = 128
    weights = pattern.astype(jnp.bfloat16)
    masked = (
        docs.reshape(doc_rows // tile_edge, tile_edge, term_cols // tile_edge, tile_edge)
        * weights[:, None, :, None]
    ).reshape(doc_rows, term_cols)
    partial_sq = jnp.einsum("dt,dt->d", masked, masked, preferred_element_type=jnp.float32)
    doc_sq = lax.psum(partial_sq, RP)
    inverse = lax.rsqrt(doc_sq + EPSILON)
    sharpen = math.sqrt(TERMS) * 0.5
    blocks = [masked[k * QUERY :][:QUERY] for k in range(doc_rows // QUERY)]
    block_of = [s % (doc_rows // QUERY) for s in range(STEPS)]
    pieces = scatter_from_owner(blocks, block_of, owners, sizes)
    piece = pieces.shape[1]
    row_share = piece // n_rep
    own_sq = lax.psum(jnp.einsum("spt,spt->sp", pieces, pieces, preferred_element_type=jnp.float32), RP)
    own_inv = lax.dynamic_slice_in_dim(lax.rsqrt(own_sq + EPSILON), rep_index * row_share, row_share, axis=1)
    flat_pieces, inverse, own_inv = lax.optimization_barrier(
        (pieces.reshape(STEPS * piece, term_cols), inverse, own_inv)
    )
    flat_queries = lax.all_gather(flat_pieces, AX, axis=0, tiled=True)
    flat_queries, stored = lax.optimization_barrier((flat_queries, masked))
    similar = lax.optimization_barrier(
        lax.dot_general(flat_queries, stored, (((1,), (1,)), ((), ())), preferred_element_type=jnp.float32)
    )
    similar = similar.reshape(n_shard, STEPS, 2, 2, row_share, doc_rows)
    similar = jnp.sum(exchange(similar, "c", 3), axis=3)
    mine = jnp.sum(exchange(similar, "zl", 2), axis=2)
    weighted = mine * inverse[None, None, None, :]
    got = exchange(weighted, AX, 0)
    scaled = got * own_inv[None, :, :, None] * sharpen
    scores = jnp.clip(scaled, -CLIP_LEVEL, CLIP_LEVEL).astype(jnp.bfloat16)
    return scores.transpose(1, 2, 0, 3).reshape(STEPS, row_share, n_shard * doc_rows)


def solution(mesh):
    names = dict(zip(("x", "z_hi", "y"), (4, 4, 4)))
    n_shard, n_rep = mesh.devices.shape
    sizes = (names["x"], names["z_hi"], names["y"])
    assert sizes[0] * sizes[1] * sizes[2] == n_shard and n_rep == 4
    mesh5 = Mesh(mesh.devices.reshape(*sizes, 2, 2), AX + RP)
    return jax.shard_map(
        lambda d, p, o: on_device(d, p, o, sizes),
        mesh=mesh5,
        in_specs=(P(AX, RP), P(AX, RP), P()),
        out_specs=P(None, AX + RP, None),
        check_vma=False,
    )
```
